32 devices in a mesh: blk: 4 (over y, x), group: 8 (over z, core).
Axes of the slice: x: 2, y: 2, z: 4, core: 2. Of those that a mesh axis runs over, the one named last changes fastest.
Arguments:
- picture_vector_list: bfloat16 [8, 1024, 768], P('group', 'blk'), may hold values from -0.25 to 0.25
- caption_latent_matrix: bfloat16 [8, 1024, 3072], P('group', 'blk'), may hold values from -6 to 6
- linear_map_matrix: bfloat16 [3072, 768], P('group'), may hold values from -0.109375 to 0.109375
- target_match_index: int32 [8, 1024], P('group', 'blk'), may hold values from 0 to 1023, each once within a row
- sharpness_factor: float32 [1], replicated, may hold values from 24 to 40
- offset_term: float32 [1], replicated, may hold values from -6 to -5
Outputs:
- row_loss: float32 [8, 1024], P('group', 'blk')
- image_grad: bfloat16 [8, 1024, 768], P('group', 'blk')
- projection_grad: float32 [3072, 768], P(('blk', 'group'))
The draws below stay inside these ranges and needn't reach their ends.
Inputs may be any that keep to these rules, and one draw needn't show every extreme that they name: `target_match_index`: each data group's row of positives is a permutation of 0 to 1023.
All inputs are finite; a program needn't handle non-finite values.
Results may differ from the reference program's by a relative error of at most 0.015.
Values may be sent and summed in bfloat16 or wider, within the bound.
No kernel may reach another device: no remote copies, remote signals or barrier semaphores. Data moves between devices by JAX's collectives and lax.ppermute only.
A program may use at most 64 MiB of HBM per device.

```python
import jax
import jax.numpy as jnp
from jax import lax

D = 768
HID = 3072
GROUP_ROWS = 1024
N_GROUP = 8


def levels(own_key, dims, split, smallest, high):
    gain, own = 1.0, jax.random.fold_in(own_key, 6)
    for axis_at, shards_of in split:
        heights = jnp.exp(jax.random.uniform(jax.random.fold_in(own, axis_at), (shards_of,), jnp.float32, smallest / len(split), high / len(split)))
        gain = gain * jnp.repeat(heights, dims[axis_at] // shards_of).reshape([-1 if axis == axis_at else 1 for axis in range(len(dims))])
    return gain


def gaussian(key, dims, width, limit, shards=(), held_as=jnp.bfloat16):
    level = levels(key, dims, shards, -0.22, 0.18) if shards else 1.0
    result = jax.random.normal(key, dims, jnp.float32) * width * level
    return jnp.minimum(jnp.maximum(result, -limit), limit).astype(held_as)


def setup_inputs(seed: int = 0) -> dict:
    splits = jax.random.split(jax.random.key(seed), 7)
    return {
        "picture_vector_list": gaussian(splits[0], (N_GROUP, GROUP_ROWS, D), 0.04, 0.25, ((0, 8), (1, 4))),
        "caption_latent_matrix": gaussian(splits[1], (N_GROUP, GROUP_ROWS, HID), 1.0, 6.0, ((0, 8), (1, 4))),
        "linear_map_matrix": gaussian(splits[2], (HID, D), HID ** -0.5, 0.109375, ((0, 8),)),
        "target_match_index": jax.vmap(lambda own: jax.random.permutation(own, GROUP_ROWS))(jax.random.split(splits[3], N_GROUP)).reshape((N_GROUP, GROUP_ROWS)).astype(jnp.int32),
        "sharpness_factor": jnp.clip(jax.random.uniform(splits[4], (1,), jnp.float32, 24.0, 40.0), 24.0, 40.0),
        "offset_term": jnp.clip(jax.random.uniform(splits[5], (1,), jnp.float32, -6.0, -5.0), -6.0, -5.0),
    }


epsilon = 1e-06

def reference(picture_vector_list, caption_latent_matrix, linear_map_matrix, target_match_index, sharpness_factor, offset_term):
    multiplier_amount = sharpness_factor[0]
    offset_value = offset_term[0]

    def one_group(carry_grad, inputs):
        image_rows, hidden_rows, label_rows = inputs
        projected = jnp.dot(hidden_rows, linear_map_matrix, preferred_element_type=jnp.float32)
        text_scale = lax.rsqrt(lax.optimization_barrier(jnp.sum(projected * projected, axis=1, keepdims=True)) + epsilon)
        text_dir = projected * text_scale
        text_unit = text_dir.astype(jnp.bfloat16)
        image_float = image_rows.astype(jnp.float32)
        image_scale = lax.rsqrt(lax.optimization_barrier(jnp.sum(image_float * image_float, axis=1, keepdims=True)) + epsilon)
        image_dir = image_float * image_scale
        image_unit = image_dir.astype(jnp.bfloat16)
        logits = multiplier_amount * jnp.dot(image_unit, text_unit.T, preferred_element_type=jnp.float32) + offset_value
        columns = jnp.arange(label_rows.shape[0], dtype=jnp.int32)
        pair_sign = jnp.where(label_rows[:, None] == columns[None, :], 1.0, -1.0).astype(jnp.float32)
        row_loss = -lax.optimization_barrier(jnp.sum(jax.nn.log_sigmoid(pair_sign * logits), axis=1))
        pair_weight = (-pair_sign * jax.nn.sigmoid(-pair_sign * logits) * multiplier_amount).astype(jnp.bfloat16)
        image_unit_grad = jnp.dot(pair_weight, text_unit, preferred_element_type=jnp.float32)
        text_unit_grad = jnp.dot(pair_weight.T, image_unit, preferred_element_type=jnp.float32)
        image_grad = (image_scale * (image_unit_grad - image_dir * lax.optimization_barrier(jnp.sum(image_dir * image_unit_grad, axis=1, keepdims=True)))).astype(jnp.bfloat16)
        projection_output_gradient = (text_scale * (text_unit_grad - text_dir * lax.optimization_barrier(jnp.sum(text_dir * text_unit_grad, axis=1, keepdims=True)))).astype(jnp.bfloat16)
        weight_grad = jnp.dot(hidden_rows.T, projection_output_gradient, preferred_element_type=jnp.float32)
        return (carry_grad + weight_grad, (row_loss, image_grad))
    start_grad = jnp.zeros(linear_map_matrix.shape, jnp.float32)
    total_grad, (losses, image_grads) = lax.scan(one_group, start_grad, (picture_vector_list, caption_latent_matrix, target_match_index))
    return (losses, image_grads, total_grad)
```

```python
import jax
import jax.numpy as jnp
from jax import lax
from jax.sharding import PartitionSpec as P

epsilon = 1e-06


def body(
    picture_vector_list,
    caption_latent_matrix,
    linear_map_matrix,
    target_match_index,
    sharpness_factor,
    offset_term,
):
    image_rows = picture_vector_list[0]
    hidden_rows = caption_latent_matrix[0]
    label_rows = target_match_index[0]
    row_count = image_rows.shape[0]
    blocks = lax.axis_size("blk")
    my_index = lax.axis_index("blk")
    multiplier_amount = sharpness_factor[0]
    offset_value = offset_term[0]

    piece_rows = linear_map_matrix.shape[0] // blocks
    w_piece = lax.dynamic_slice_in_dim(linear_map_matrix, my_index * piece_rows, piece_rows, 0)
    w_full = lax.all_gather(w_piece, ("group", "blk"), axis=0, tiled=True)

    hidden_chunk = lax.all_to_all(hidden_rows, "blk", split_axis=1, concat_axis=0, tiled=True)

    image_float = image_rows.astype(jnp.float32)
    image_scale = lax.rsqrt(jnp.sum(image_float * image_float, axis=1, keepdims=True) + epsilon)
    image_dir = image_float * image_scale
    image_unit = image_dir.astype(jnp.bfloat16)

    projected = jnp.dot(hidden_rows, w_full, preferred_element_type=jnp.float32)
    text_scale = lax.rsqrt(jnp.sum(projected * projected, axis=1, keepdims=True) + epsilon)
    text_dir = projected * text_scale
    text_unit = text_dir.astype(jnp.bfloat16)

    both = lax.all_gather(jnp.stack([image_unit, text_unit]), "blk", axis=1, tiled=True)
    image_all = both[0]
    text_all = both[1]
    label_all = lax.all_gather(label_rows.astype(jnp.float32), "blk", axis=0, tiled=True)

    def weights_of(logits, pair_sign):
        return (-pair_sign * jax.nn.sigmoid(-pair_sign * logits) * multiplier_amount).astype(
            jnp.bfloat16
        )

    scores = lax.dot_general(
        image_unit, text_all, (((1,), (1,)), ((), ())), preferred_element_type=jnp.float32
    )
    logits = multiplier_amount * scores + offset_value
    text_columns = jnp.arange(text_all.shape[0], dtype=jnp.int32)
    pair_sign = jnp.where(label_rows[:, None] == text_columns[None, :], 1.0, -1.0).astype(
        jnp.float32
    )
    loss_local = -jnp.sum(jax.nn.log_sigmoid(pair_sign * logits), axis=1)
    image_unit_grad = jnp.dot(
        weights_of(logits, pair_sign), text_all, preferred_element_type=jnp.float32
    )

    scores_t = lax.dot_general(
        image_all, text_unit, (((1,), (1,)), ((), ())), preferred_element_type=jnp.float32
    )
    logits_t = multiplier_amount * scores_t + offset_value
    own_columns = (my_index * row_count + jnp.arange(row_count, dtype=jnp.int32)).astype(
        jnp.float32
    )
    pair_sign_t = jnp.where(label_all[:, None] == own_columns[None, :], 1.0, -1.0).astype(
        jnp.float32
    )
    text_unit_grad = lax.dot_general(
        weights_of(logits_t, pair_sign_t),
        image_all,
        (((0,), (0,)), ((), ())),
        preferred_element_type=jnp.float32,
    )

    image_grad = (
        image_scale
        * (
            image_unit_grad
            - image_dir * jnp.sum(image_dir * image_unit_grad, axis=1, keepdims=True)
        )
    ).astype(jnp.bfloat16)
    projection_output_gradient = (
        text_scale
        * (text_unit_grad - text_dir * jnp.sum(text_dir * text_unit_grad, axis=1, keepdims=True))
    ).astype(jnp.bfloat16)

    grad_all = lax.all_gather(projection_output_gradient, "blk", axis=0, tiled=True)
    partial = lax.dot_general(
        hidden_chunk, grad_all, (((0,), (0,)), ((), ())), preferred_element_type=jnp.float32
    )
    projection_grad = lax.psum_scatter(partial, "group", scatter_dimension=0, tiled=True)
    return (loss_local[None], image_grad[None], projection_grad)


def solution(mesh):
    return jax.shard_map(
        body,
        mesh=mesh,
        in_specs=(
            P("group", "blk", None),
            P("group", "blk", None),
            P("group", None),
            P("group", "blk"),
            P(),
            P(),
        ),
        out_specs=(P("group", "blk"), P("group", "blk", None), P(("blk", "group"), None)),
        check_vma=False,
    )
```

```python
import jax
import jax.numpy as jnp
from jax import lax
from jax.sharding import PartitionSpec as P

epsilon = 1e-06


def partner_pairs(count, step):
    if count & (count - 1) == 0:
        return [(source, source ^ step) for source in range(count)]
    return [(source, (source + step) % count) for source in range(count)]


def partner_of(index, count, step):
    if count & (count - 1) == 0:
        return index ^ step
    return (index - step) % count


def body(
    picture_vector_list,
    caption_latent_matrix,
    linear_map_matrix,
    target_match_index,
    sharpness_factor,
    offset_term,
):
    image_rows = picture_vector_list[0]
    hidden_rows = caption_latent_matrix[0]
    label_rows = target_match_index[0]
    row_count = image_rows.shape[0]
    hid = hidden_rows.shape[1]
    blocks = lax.axis_size("blk")
    my_index = lax.axis_index("blk")
    chunk = hid // blocks
    multiplier_amount = sharpness_factor[0]
    offset_value = offset_term[0]

    def exchange(value, step):
        return lax.ppermute(value, "blk", partner_pairs(blocks, step))

    w_full = lax.all_gather(linear_map_matrix, "group", axis=0, tiled=True)

    image_float = image_rows.astype(jnp.float32)
    image_scale = lax.rsqrt(jnp.sum(image_float * image_float, axis=1, keepdims=True) + epsilon)
    image_dir = image_float * image_scale
    image_unit = image_dir.astype(jnp.bfloat16)

    source = [my_index] + [partner_of(my_index, blocks, k) for k in range(1, blocks)]
    own_hidden_chunk = lax.dynamic_slice_in_dim(hidden_rows, my_index * chunk, chunk, 1)
    hidden_from = [own_hidden_chunk]
    image_from = [image_unit]
    label_from = [label_rows]
    for k in range(1, blocks):
        target = partner_of(my_index, blocks, k)
        outgoing = jnp.concatenate(
            [lax.dynamic_slice_in_dim(hidden_rows, target * chunk, chunk, 1), image_unit], axis=1
        )
        incoming = exchange(outgoing, k)
        hidden_from.append(incoming[:, :chunk])
        image_from.append(incoming[:, chunk:])
        label_from.append(exchange(label_rows, k))

    projected = jnp.dot(hidden_rows, w_full, preferred_element_type=jnp.float32)
    text_scale = lax.rsqrt(jnp.sum(projected * projected, axis=1, keepdims=True) + epsilon)
    text_dir = projected * text_scale
    text_unit = text_dir.astype(jnp.bfloat16)
    text_from = [text_unit] + [exchange(text_unit, k) for k in range(1, blocks)]

    def weights_of(logits, pair_sign):
        return (-pair_sign * jax.nn.sigmoid(-pair_sign * logits) * multiplier_amount).astype(
            jnp.bfloat16
        )

    local = jnp.arange(row_count, dtype=jnp.int32)

    own_columns = my_index * row_count + local
    text_unit_grad = jnp.zeros(text_unit.shape, jnp.float32)
    for k in range(blocks):
        scores_t = lax.dot_general(
            image_from[k], text_unit, (((1,), (1,)), ((), ())), preferred_element_type=jnp.float32
        )
        logits_t = multiplier_amount * scores_t + offset_value
        pair_sign_t = jnp.where(label_from[k][:, None] == own_columns[None, :], 1.0, -1.0).astype(
            jnp.float32
        )
        text_unit_grad = text_unit_grad + lax.dot_general(
            weights_of(logits_t, pair_sign_t),
            image_from[k],
            (((0,), (0,)), ((), ())),
            preferred_element_type=jnp.float32,
        )
    projection_output_gradient = (
        text_scale
        * (text_unit_grad - text_dir * jnp.sum(text_dir * text_unit_grad, axis=1, keepdims=True))
    ).astype(jnp.bfloat16)
    grad_from = [projection_output_gradient] + [
        exchange(projection_output_gradient, k) for k in range(1, blocks)
    ]
    partial = jnp.zeros((chunk, projection_output_gradient.shape[1]), jnp.float32)
    for k in range(blocks):
        partial = partial + lax.dot_general(
            hidden_from[k], grad_from[k], (((0,), (0,)), ((), ())), preferred_element_type=jnp.float32
        )
    projection_grad = lax.psum_scatter(partial, "group", scatter_dimension=0, tiled=True)

    loss_local = jnp.zeros((row_count,), jnp.float32)
    image_unit_grad = jnp.zeros(image_unit.shape, jnp.float32)
    for k in range(blocks):
        scores = lax.dot_general(
            image_unit, text_from[k], (((1,), (1,)), ((), ())), preferred_element_type=jnp.float32
        )
        logits = multiplier_amount * scores + offset_value
        columns = source[k] * row_count + local
        pair_sign = jnp.where(label_rows[:, None] == columns[None, :], 1.0, -1.0).astype(
            jnp.float32
        )
        loss_local = loss_local + -jnp.sum(jax.nn.log_sigmoid(pair_sign * logits), axis=1)
        image_unit_grad = image_unit_grad + jnp.dot(
            weights_of(logits, pair_sign), text_from[k], preferred_element_type=jnp.float32
        )
    image_grad = (
        image_scale
        * (
            image_unit_grad
            - image_dir * jnp.sum(image_dir * image_unit_grad, axis=1, keepdims=True)
        )
    ).astype(jnp.bfloat16)
    return (loss_local[None], image_grad[None], projection_grad)


def solution(mesh):
    return jax.shard_map(
        body,
        mesh=mesh,
        in_specs=(
            P("group", "blk", None),
            P("group", "blk", None),
            P("group", None),
            P("group", "blk"),
            P(),
            P(),
        ),
        out_specs=(P("group", "blk"), P("group", "blk", None), P(("blk", "group"), None)),
        check_vma=False,
    )
```

```python
import jax
import jax.numpy as jnp
from jax import lax
from jax.sharding import PartitionSpec as P

epsilon = 1e-06


def partner_pairs(count, step):
    if count & (count - 1) == 0:
        return [(source, source ^ step) for source in range(count)]
    return [(source, (source + step) % count) for source in range(count)]


def partner_of(index, count, step):
    if count & (count - 1) == 0:
        return index ^ step
    return (index - step) % count


def body(
    picture_vector_list,
    caption_latent_matrix,
    linear_map_matrix,
    target_match_index,
    sharpness_factor,
    offset_term,
):
    image_rows = picture_vector_list[0]
    hidden_rows = caption_latent_matrix[0]
    label_rows = target_match_index[0]
    row_count = image_rows.shape[0]
    hid = hidden_rows.shape[1]
    blocks = lax.axis_size("blk")
    my_index = lax.axis_index("blk")
    chunk = hid // blocks
    multiplier_amount = sharpness_factor[0]
    offset_value = offset_term[0]

    def exchange(value, step):
        return lax.ppermute(value, "blk", partner_pairs(blocks, step))

    shard_rows = linear_map_matrix.shape[0]
    piece_rows = shard_rows // blocks
    groups = lax.axis_size("group")
    w_piece = lax.dynamic_slice_in_dim(linear_map_matrix, my_index * piece_rows, piece_rows, 0)
    w_quarter = lax.all_gather(w_piece, "group", axis=0, tiled=False)
    w_parts = jnp.zeros((groups, blocks, piece_rows, w_piece.shape[1]), w_piece.dtype)
    w_parts = lax.dynamic_update_slice_in_dim(w_parts, w_quarter[:, None], my_index, 1)
    for k in range(1, blocks):
        w_parts = lax.dynamic_update_slice_in_dim(
            w_parts, exchange(w_quarter, k)[:, None], partner_of(my_index, blocks, k), 1
        )
    w_full = w_parts.reshape(groups * shard_rows, w_piece.shape[1])

    image_float = image_rows.astype(jnp.float32)
    image_scale = lax.rsqrt(jnp.sum(image_float * image_float, axis=1, keepdims=True) + epsilon)
    image_dir = image_float * image_scale
    image_unit = image_dir.astype(jnp.bfloat16)

    source = [my_index] + [partner_of(my_index, blocks, k) for k in range(1, blocks)]
    own_hidden_chunk = lax.dynamic_slice_in_dim(hidden_rows, my_index * chunk, chunk, 1)
    hidden_from = [own_hidden_chunk]
    image_from = [image_unit]
    label_from = [label_rows]
    for k in range(1, blocks):
        target = partner_of(my_index, blocks, k)
        outgoing, _ = lax.optimization_barrier(
            (lax.dynamic_slice_in_dim(hidden_rows, target * chunk, chunk, 1), w_full)
        )
        hidden_from.append(exchange(outgoing, k))
        image_from.append(exchange(image_unit, k))
        label_from.append(exchange(label_rows, k))

    projected = jnp.dot(hidden_rows, w_full, preferred_element_type=jnp.float32)
    text_scale = lax.rsqrt(jnp.sum(projected * projected, axis=1, keepdims=True) + epsilon)
    text_dir = projected * text_scale
    text_unit = text_dir.astype(jnp.bfloat16)
    text_from = [text_unit] + [exchange(text_unit, k) for k in range(1, blocks)]

    def weights_of(logits, pair_sign):
        return (-pair_sign * jax.nn.sigmoid(-pair_sign * logits) * multiplier_amount).astype(
            jnp.bfloat16
        )

    local = jnp.arange(row_count, dtype=jnp.int32)

    own_columns = my_index * row_count + local
    text_unit_grad = jnp.zeros(text_unit.shape, jnp.float32)
    for k in range(blocks):
        scores_t = lax.dot_general(
            image_from[k], text_unit, (((1,), (1,)), ((), ())), preferred_element_type=jnp.float32
        )
        logits_t = multiplier_amount * scores_t + offset_value
        pair_sign_t = jnp.where(label_from[k][:, None] == own_columns[None, :], 1.0, -1.0).astype(
            jnp.float32
        )
        text_unit_grad = text_unit_grad + lax.dot_general(
            weights_of(logits_t, pair_sign_t),
            image_from[k],
            (((0,), (0,)), ((), ())),
            preferred_element_type=jnp.float32,
        )
    projection_output_gradient = (
        text_scale
        * (text_unit_grad - text_dir * jnp.sum(text_dir * text_unit_grad, axis=1, keepdims=True))
    ).astype(jnp.bfloat16)
    grad_send, hidden_remote = lax.optimization_barrier(
        (projection_output_gradient, hidden_from[1:])
    )
    hidden_from = hidden_from[:1] + list(hidden_remote)
    grad_from = [projection_output_gradient] + [exchange(grad_send, k) for k in range(1, blocks)]
    partial = jnp.zeros((chunk, projection_output_gradient.shape[1]), jnp.float32)
    for k in range(blocks):
        partial = partial + lax.dot_general(
            hidden_from[k], grad_from[k], (((0,), (0,)), ((), ())), preferred_element_type=jnp.float32
        )
    projection_grad = lax.psum_scatter(partial, "group", scatter_dimension=0, tiled=True)

    loss_local = jnp.zeros((row_count,), jnp.float32)
    image_unit_grad = jnp.zeros(image_unit.shape, jnp.float32)
    for k in range(blocks):
        scores = lax.dot_general(
            image_unit, text_from[k], (((1,), (1,)), ((), ())), preferred_element_type=jnp.float32
        )
        logits = multiplier_amount * scores + offset_value
        columns = source[k] * row_count + local
        pair_sign = jnp.where(label_rows[:, None] == columns[None, :], 1.0, -1.0).astype(
            jnp.float32
        )
        loss_local = loss_local + -jnp.sum(jax.nn.log_sigmoid(pair_sign * logits), axis=1)
        image_unit_grad = image_unit_grad + jnp.dot(
            weights_of(logits, pair_sign), text_from[k], preferred_element_type=jnp.float32
        )
    image_grad = (
        image_scale
        * (
            image_unit_grad
            - image_dir * jnp.sum(image_dir * image_unit_grad, axis=1, keepdims=True)
        )
    ).astype(jnp.bfloat16)
    return (loss_local[None], image_grad[None], projection_grad)


def solution(mesh):
    return jax.shard_map(
        body,
        mesh=mesh,
        in_specs=(
            P("group", "blk", None),
            P("group", "blk", None),
            P("group", None),
            P("group", "blk"),
            P(),
            P(),
        ),
        out_specs=(P("group", "blk"), P("group", "blk", None), P(("blk", "group"), None)),
        check_vma=False,
    )
```

```python
import jax
import jax.numpy as jnp
from jax import lax
from jax.sharding import PartitionSpec as P

epsilon = 1e-06


def partner_pairs(count, step):
    if count & (count - 1) == 0:
        return [(source, source ^ step) for source in range(count)]
    return [(source, (source + step) % count) for source in range(count)]


def partner_of(index, count, step):
    if count & (count - 1) == 0:
        return index ^ step
    return (index - step) % count


def body(
    picture_vector_list,
    caption_latent_matrix,
    linear_map_matrix,
    target_match_index,
    sharpness_factor,
    offset_term,
):
    image_rows = picture_vector_list[0]
    hidden_rows = caption_latent_matrix[0]
    label_rows = target_match_index[0]
    row_count = image_rows.shape[0]
    hid = hidden_rows.shape[1]
    blocks = lax.axis_size("blk")
    my_index = lax.axis_index("blk")
    chunk = hid // blocks
    multiplier_amount = sharpness_factor[0]
    offset_value = offset_term[0]

    def exchange(value, step):
        return lax.ppermute(value, "blk", partner_pairs(blocks, step))

    w_full = lax.all_gather(linear_map_matrix, "group", axis=0, tiled=True)

    image_float = image_rows.astype(jnp.float32)
    image_scale = lax.rsqrt(jnp.sum(image_float * image_float, axis=1, keepdims=True) + epsilon)
    image_dir = image_float * image_scale
    image_unit = image_dir.astype(jnp.bfloat16)

    source = [my_index] + [partner_of(my_index, blocks, k) for k in range(1, blocks)]
    own_hidden_chunk = lax.dynamic_slice_in_dim(hidden_rows, my_index * chunk, chunk, 1)
    hidden_from = [own_hidden_chunk]
    image_from = [image_unit]
    label_from = [label_rows]
    for k in range(1, blocks):
        target = partner_of(my_index, blocks, k)
        outgoing = jnp.concatenate(
            [lax.dynamic_slice_in_dim(hidden_rows, target * chunk, chunk, 1), image_unit], axis=1
        )
        incoming = exchange(outgoing, k)
        hidden_from.append(incoming[:, :chunk])
        image_from.append(incoming[:, chunk:])
        label_from.append(exchange(label_rows, k))

    projected = jnp.dot(hidden_rows, w_full, preferred_element_type=jnp.float32)
    text_scale = lax.rsqrt(jnp.sum(projected * projected, axis=1, keepdims=True) + epsilon)
    text_dir = projected * text_scale
    text_unit = text_dir.astype(jnp.bfloat16)
    text_from = [text_unit] + [exchange(text_unit, k) for k in range(1, blocks)]

    def weights_of(logits, pair_sign):
        return (-pair_sign * jax.nn.sigmoid(-pair_sign * logits) * multiplier_amount).astype(
            jnp.bfloat16
        )

    local = jnp.arange(row_count, dtype=jnp.int32)

    image_group = jnp.concatenate(image_from, axis=0)
    label_group = jnp.concatenate(label_from, axis=0)
    hidden_group = jnp.concatenate(hidden_from, axis=0)
    own_columns = my_index * row_count + local
    scores_t = lax.dot_general(
        image_group, text_unit, (((1,), (1,)), ((), ())), preferred_element_type=jnp.float32
    )
    logits_t = multiplier_amount * scores_t + offset_value
    pair_sign_t = jnp.where(label_group[:, None] == own_columns[None, :], 1.0, -1.0).astype(
        jnp.float32
    )
    text_unit_grad = lax.dot_general(
        weights_of(logits_t, pair_sign_t),
        image_group,
        (((0,), (0,)), ((), ())),
        preferred_element_type=jnp.float32,
    )
    projection_output_gradient = (
        text_scale
        * (text_unit_grad - text_dir * jnp.sum(text_dir * text_unit_grad, axis=1, keepdims=True))
    ).astype(jnp.bfloat16)
    grad_from = [projection_output_gradient] + [
        exchange(projection_output_gradient, k) for k in range(1, blocks)
    ]
    partial = lax.dot_general(
        hidden_group,
        jnp.concatenate(grad_from, axis=0),
        (((0,), (0,)), ((), ())),
        preferred_element_type=jnp.float32,
    )
    projection_grad = lax.psum_scatter(partial, "group", scatter_dimension=0, tiled=True)

    loss_local = jnp.zeros((row_count,), jnp.float32)
    image_unit_grad = jnp.zeros(image_unit.shape, jnp.float32)
    for k in range(blocks):
        scores = lax.dot_general(
            image_unit, text_from[k], (((1,), (1,)), ((), ())), preferred_element_type=jnp.float32
        )
        logits = multiplier_amount * scores + offset_value
        columns = source[k] * row_count + local
        pair_sign = jnp.where(label_rows[:, None] == columns[None, :], 1.0, -1.0).astype(
            jnp.float32
        )
        loss_local = loss_local + -jnp.sum(jax.nn.log_sigmoid(pair_sign * logits), axis=1)
        image_unit_grad = image_unit_grad + jnp.dot(
            weights_of(logits, pair_sign), text_from[k], preferred_element_type=jnp.float32
        )
    image_grad = (
        image_scale
        * (
            image_unit_grad
            - image_dir * jnp.sum(image_dir * image_unit_grad, axis=1, keepdims=True)
        )
    ).astype(jnp.bfloat16)
    return (loss_local[None], image_grad[None], projection_grad)


def solution(mesh):
    return jax.shard_map(
        body,
        mesh=mesh,
        in_specs=(
            P("group", "blk", None),
            P("group", "blk", None),
            P("group", None),
            P("group", "blk"),
            P(),
            P(),
        ),
        out_specs=(P("group", "blk"), P("group", "blk", None), P(("blk", "group"), None)),
        check_vma=False,
    )
```

```python
import jax
import jax.numpy as jnp
from jax import lax
from jax.sharding import PartitionSpec as P

epsilon = 1e-06


def partner_pairs(count, step):
    if count & (count - 1) == 0:
        return [(source, source ^ step) for source in range(count)]
    return [(source, (source + step) % count) for source in range(count)]


def partner_of(index, count, step):
    if count & (count - 1) == 0:
        return index ^ step
    return (index - step) % count


def body(
    picture_vector_list,
    caption_latent_matrix,
    linear_map_matrix,
    target_match_index,
    sharpness_factor,
    offset_term,
):
    image_rows = picture_vector_list[0]
    hidden_rows = caption_latent_matrix[0]
    label_rows = target_match_index[0]
    row_count = image_rows.shape[0]
    hid = hidden_rows.shape[1]
    blocks = lax.axis_size("blk")
    my_index = lax.axis_index("blk")
    chunk = hid // blocks
    multiplier_amount = sharpness_factor[0]
    offset_value = offset_term[0]

    def exchange(value, step):
        return lax.ppermute(value, "blk", partner_pairs(blocks, step))

    w_full = lax.all_gather(linear_map_matrix, "group", axis=0, tiled=True)

    image_float = image_rows.astype(jnp.float32)
    image_scale = lax.rsqrt(jnp.sum(image_float * image_float, axis=1, keepdims=True) + epsilon)
    image_dir = image_float * image_scale
    image_unit = image_dir.astype(jnp.bfloat16)

    source = [my_index] + [partner_of(my_index, blocks, k) for k in range(1, blocks)]
    own_hidden_chunk = lax.dynamic_slice_in_dim(hidden_rows, my_index * chunk, chunk, 1)
    hidden_from = [own_hidden_chunk]
    image_from = [image_unit]
    label_from = [label_rows]
    for k in range(1, blocks):
        target = partner_of(my_index, blocks, k)
        outgoing = jnp.concatenate(
            [lax.dynamic_slice_in_dim(hidden_rows, target * chunk, chunk, 1), image_unit], axis=1
        )
        incoming = exchange(outgoing, k)
        hidden_from.append(incoming[:, :chunk])
        image_from.append(incoming[:, chunk:])
        label_from.append(exchange(label_rows, k))

    projected = jnp.dot(hidden_rows, w_full, preferred_element_type=jnp.float32)
    text_scale = lax.rsqrt(jnp.sum(projected * projected, axis=1, keepdims=True) + epsilon)
    text_dir = projected * text_scale
    text_unit = text_dir.astype(jnp.bfloat16)
    text_from = [text_unit] + [exchange(text_unit, k) for k in range(1, blocks)]

    def weights_of(logits, pair_sign):
        return (-pair_sign * jax.nn.sigmoid(-pair_sign * logits) * multiplier_amount).astype(
            jnp.bfloat16
        )

    local = jnp.arange(row_count, dtype=jnp.int32)

    image_group = jnp.concatenate(image_from, axis=0)
    label_group = jnp.concatenate(label_from, axis=0)
    halves = 2 if row_count % 16 == 0 else 1
    half_rows = row_count // halves
    partial = None
    for h in range(halves):
        rows = slice(h * half_rows, (h + 1) * half_rows)
        text_part = text_unit[rows]
        dir_part = text_dir[rows]
        own_columns = my_index * row_count + h * half_rows + local[:half_rows]
        scores_t = lax.dot_general(
            image_group, text_part, (((1,), (1,)), ((), ())), preferred_element_type=jnp.float32
        )
        logits_t = multiplier_amount * scores_t + offset_value
        pair_sign_t = jnp.where(label_group[:, None] == own_columns[None, :], 1.0, -1.0).astype(
            jnp.float32
        )
        text_unit_grad = lax.dot_general(
            weights_of(logits_t, pair_sign_t),
            image_group,
            (((0,), (0,)), ((), ())),
            preferred_element_type=jnp.float32,
        )
        projection_output_gradient = (
            text_scale[rows]
            * (text_unit_grad - dir_part * jnp.sum(dir_part * text_unit_grad, axis=1, keepdims=True))
        ).astype(jnp.bfloat16)
        grad_from = [projection_output_gradient] + [
            exchange(projection_output_gradient, k) for k in range(1, blocks)
        ]
        hidden_part = jnp.concatenate([block[rows] for block in hidden_from], axis=0)
        term = lax.dot_general(
            hidden_part,
            jnp.concatenate(grad_from, axis=0),
            (((0,), (0,)), ((), ())),
            preferred_element_type=jnp.float32,
        )
        partial = term if partial is None else partial + term
    projection_grad = lax.psum_scatter(partial, "group", scatter_dimension=0, tiled=True)

    loss_local = jnp.zeros((row_count,), jnp.float32)
    image_unit_grad = jnp.zeros(image_unit.shape, jnp.float32)
    for k in range(blocks):
        scores = lax.dot_general(
            image_unit, text_from[k], (((1,), (1,)), ((), ())), preferred_element_type=jnp.float32
        )
        logits = multiplier_amount * scores + offset_value
        columns = source[k] * row_count + local
        pair_sign = jnp.where(label_rows[:, None] == columns[None, :], 1.0, -1.0).astype(
            jnp.float32
        )
        loss_local = loss_local + -jnp.sum(jax.nn.log_sigmoid(pair_sign * logits), axis=1)
        image_unit_grad = image_unit_grad + jnp.dot(
            weights_of(logits, pair_sign), text_from[k], preferred_element_type=jnp.float32
        )
    image_grad = (
        image_scale
        * (
            image_unit_grad
            - image_dir * jnp.sum(image_dir * image_unit_grad, axis=1, keepdims=True)
        )
    ).astype(jnp.bfloat16)
    return (loss_local[None], image_grad[None], projection_grad)


def solution(mesh):
    return jax.shard_map(
        body,
        mesh=mesh,
        in_specs=(
            P("group", "blk", None),
            P("group", "blk", None),
            P("group", None),
            P("group", "blk"),
            P(),
            P(),
        ),
        out_specs=(P("group", "blk"), P("group", "blk", None), P(("blk", "group"), None)),
        check_vma=False,
    )
```

```python
import jax
import jax.numpy as jnp
from jax import lax
from jax.sharding import PartitionSpec as P

epsilon = 1e-06


def partner_pairs(count, step):
    if count & (count - 1) == 0:
        return [(source, source ^ step) for source in range(count)]
    return [(source, (source + step) % count) for source in range(count)]


def partner_of(index, count, step):
    if count & (count - 1) == 0:
        return index ^ step
    return (index - step) % count


def body(
    picture_vector_list,
    caption_latent_matrix,
    linear_map_matrix,
    target_match_index,
    sharpness_factor,
    offset_term,
):
    image_rows = picture_vector_list[0]
    hidden_rows = caption_latent_matrix[0]
    label_rows = target_match_index[0]
    row_count = image_rows.shape[0]
    hid = hidden_rows.shape[1]
    blocks = lax.axis_size("blk")
    my_index = lax.axis_index("blk")
    chunk = hid // blocks
    multiplier_amount = sharpness_factor[0]
    offset_value = offset_term[0]

    def exchange(value, step):
        return lax.ppermute(value, "blk", partner_pairs(blocks, step))

    w_full = lax.all_gather(linear_map_matrix, "group", axis=0, tiled=True)

    image_float = image_rows.astype(jnp.float32)
    image_scale = lax.rsqrt(jnp.sum(image_float * image_float, axis=1, keepdims=True) + epsilon)
    image_dir = image_float * image_scale
    image_unit = image_dir.astype(jnp.bfloat16)

    source = [my_index] + [partner_of(my_index, blocks, k) for k in range(1, blocks)]
    own_hidden_chunk = lax.dynamic_slice_in_dim(hidden_rows, my_index * chunk, chunk, 1)
    hidden_from = [own_hidden_chunk]
    image_from = [image_unit]
    label_from = [label_rows]
    for k in range(1, blocks):
        target = partner_of(my_index, blocks, k)
        outgoing = jnp.concatenate(
            [lax.dynamic_slice_in_dim(hidden_rows, target * chunk, chunk, 1), image_unit], axis=1
        )
        incoming = exchange(outgoing, k)
        hidden_from.append(incoming[:, :chunk])
        image_from.append(incoming[:, chunk:])
        label_from.append(exchange(label_rows, k))

    projected = jnp.dot(hidden_rows, w_full, preferred_element_type=jnp.float32)
    text_scale = lax.rsqrt(jnp.sum(projected * projected, axis=1, keepdims=True) + epsilon)
    text_dir = projected * text_scale
    text_unit = text_dir.astype(jnp.bfloat16)
    text_from = [text_unit] + [exchange(text_unit, k) for k in range(1, blocks)]

    def weights_of(logits, pair_sign):
        return (-pair_sign * jax.nn.sigmoid(-pair_sign * logits) * multiplier_amount).astype(
            jnp.bfloat16
        )

    local = jnp.arange(row_count, dtype=jnp.int32)

    image_group = jnp.concatenate(image_from, axis=0)
    label_group = jnp.concatenate(label_from, axis=0)
    hidden_group = jnp.concatenate(hidden_from, axis=0)
    own_columns = my_index * row_count + local
    scores_t = lax.dot_general(
        image_group, text_unit, (((1,), (1,)), ((), ())), preferred_element_type=jnp.float32
    )
    logits_t = multiplier_amount * scores_t + offset_value
    pair_sign_t = jnp.where(label_group[:, None] == own_columns[None, :], 1.0, -1.0).astype(
        jnp.float32
    )
    text_unit_grad = lax.dot_general(
        weights_of(logits_t, pair_sign_t),
        image_group,
        (((0,), (0,)), ((), ())),
        preferred_element_type=jnp.float32,
    )
    projection_output_gradient = (
        text_scale
        * (text_unit_grad - text_dir * jnp.sum(text_dir * text_unit_grad, axis=1, keepdims=True))
    ).astype(jnp.bfloat16)
    grad_from = [projection_output_gradient] + [
        exchange(projection_output_gradient, k) for k in range(1, blocks)
    ]
    partial = lax.dot_general(
        hidden_group,
        jnp.concatenate(grad_from, axis=0),
        (((0,), (0,)), ((), ())),
        preferred_element_type=jnp.float32,
    )
    projection_grad = lax.psum_scatter(
        partial.astype(jnp.bfloat16), "group", scatter_dimension=0, tiled=True
    ).astype(jnp.float32)

    loss_local = jnp.zeros((row_count,), jnp.float32)
    image_unit_grad = jnp.zeros(image_unit.shape, jnp.float32)
    for k in range(blocks):
        scores = lax.dot_general(
            image_unit, text_from[k], (((1,), (1,)), ((), ())), preferred_element_type=jnp.float32
        )
        logits = multiplier_amount * scores + offset_value
        columns = source[k] * row_count + local
        pair_sign = jnp.where(label_rows[:, None] == columns[None, :], 1.0, -1.0).astype(
            jnp.float32
        )
        loss_local = loss_local + -jnp.sum(jax.nn.log_sigmoid(pair_sign * logits), axis=1)
        image_unit_grad = image_unit_grad + jnp.dot(
            weights_of(logits, pair_sign), text_from[k], preferred_element_type=jnp.float32
        )
    image_grad = (
        image_scale
        * (
            image_unit_grad
            - image_dir * jnp.sum(image_dir * image_unit_grad, axis=1, keepdims=True)
        )
    ).astype(jnp.bfloat16)
    return (loss_local[None], image_grad[None], projection_grad)


def solution(mesh):
    return jax.shard_map(
        body,
        mesh=mesh,
        in_specs=(
            P("group", "blk", None),
            P("group", "blk", None),
            P("group", None),
            P("group", "blk"),
            P(),
            P(),
        ),
        out_specs=(P("group", "blk"), P("group", "blk", None), P(("blk", "group"), None)),
        check_vma=False,
    )
```

```python
import jax
import jax.numpy as jnp
from jax import lax
from jax.sharding import PartitionSpec as P

epsilon = 1e-06


def partner_pairs(count, step):
    if count & (count - 1) == 0:
        return [(source, source ^ step) for source in range(count)]
    return [(source, (source + step) % count) for source in range(count)]


def partner_of(index, count, step):
    if count & (count - 1) == 0:
        return index ^ step
    return (index - step) % count


def body(
    picture_vector_list,
    caption_latent_matrix,
    linear_map_matrix,
    target_match_index,
    sharpness_factor,
    offset_term,
):
    image_rows = picture_vector_list[0]
    hidden_rows = caption_latent_matrix[0]
    label_rows = target_match_index[0]
    row_count = image_rows.shape[0]
    hid = hidden_rows.shape[1]
    blocks = lax.axis_size("blk")
    my_index = lax.axis_index("blk")
    chunk = hid // blocks
    multiplier_amount = sharpness_factor[0]
    offset_value = offset_term[0]

    def exchange(value, step):
        return lax.ppermute(value, "blk", partner_pairs(blocks, step))

    w_full = lax.all_gather(linear_map_matrix, "group", axis=0, tiled=True)

    image_float = image_rows.astype(jnp.float32)
    image_scale = lax.rsqrt(jnp.sum(image_float * image_float, axis=1, keepdims=True) + epsilon)
    image_dir = image_float * image_scale
    image_unit = image_dir.astype(jnp.bfloat16)

    source = [my_index] + [partner_of(my_index, blocks, k) for k in range(1, blocks)]
    own_hidden_chunk = lax.dynamic_slice_in_dim(hidden_rows, my_index * chunk, chunk, 1)
    hidden_from = [own_hidden_chunk]
    image_from = [image_unit]
    label_from = [label_rows]
    for k in range(1, blocks):
        target = partner_of(my_index, blocks, k)
        outgoing = jnp.concatenate(
            [lax.dynamic_slice_in_dim(hidden_rows, target * chunk, chunk, 1), image_unit], axis=1
        )
        incoming = exchange(outgoing, k)
        hidden_from.append(incoming[:, :chunk])
        image_from.append(incoming[:, chunk:])
        label_from.append(exchange(label_rows, k))

    projected = jnp.dot(hidden_rows, w_full, preferred_element_type=jnp.float32)
    text_scale = lax.rsqrt(jnp.sum(projected * projected, axis=1, keepdims=True) + epsilon)
    text_dir = projected * text_scale
    text_unit = text_dir.astype(jnp.bfloat16)
    text_from = [text_unit] + [exchange(text_unit, k) for k in range(1, blocks)]

    def weights_of(logits, pair_sign):
        return (-pair_sign * jax.nn.sigmoid(-pair_sign * logits) * multiplier_amount).astype(
            jnp.bfloat16
        )

    local = jnp.arange(row_count, dtype=jnp.int32)

    image_group = jnp.concatenate(image_from, axis=0)
    label_group = jnp.concatenate(label_from, axis=0)
    hidden_group = jnp.concatenate(hidden_from, axis=0)
    own_columns = my_index * row_count + local
    scores_t = lax.dot_general(
        image_group, text_unit, (((1,), (1,)), ((), ())), preferred_element_type=jnp.float32
    )
    logits_t = multiplier_amount * scores_t + offset_value
    pair_sign_t = jnp.where(label_group[:, None] == own_columns[None, :], 1.0, -1.0).astype(
        jnp.float32
    )
    text_unit_grad = lax.dot_general(
        weights_of(logits_t, pair_sign_t),
        image_group,
        (((0,), (0,)), ((), ())),
        preferred_element_type=jnp.float32,
    )
    projection_output_gradient = (
        text_scale
        * (text_unit_grad - text_dir * jnp.sum(text_dir * text_unit_grad, axis=1, keepdims=True))
    ).astype(jnp.bfloat16)
    grad_from = [projection_output_gradient] + [
        exchange(projection_output_gradient, k) for k in range(1, blocks)
    ]
    partial = lax.dot_general(
        hidden_group,
        jnp.concatenate(grad_from, axis=0),
        (((0,), (0,)), ((), ())),
        preferred_element_type=jnp.float32,
    )
    groups = lax.axis_size("group")
    parity = lax.axis_index("group") % 2
    by_owner = partial.reshape(groups // 2, 2, partial.shape[0] // groups, partial.shape[1])
    keep = lax.dynamic_index_in_dim(by_owner, parity, 1, keepdims=False)
    give = lax.dynamic_index_in_dim(by_owner, 1 - parity, 1, keepdims=False)
    mate_pairs = [(g, g ^ 1) for g in range(groups)]
    chip_sum = keep + lax.ppermute(give, "group", mate_pairs)
    same_core = [list(range(p, groups, 2)) for p in range(2)]
    projection_grad = lax.psum_scatter(
        chip_sum, "group", scatter_dimension=0, axis_index_groups=same_core, tiled=True
    ).reshape(partial.shape[0] // groups, partial.shape[1])

    loss_local = jnp.zeros((row_count,), jnp.float32)
    image_unit_grad = jnp.zeros(image_unit.shape, jnp.float32)
    for k in range(blocks):
        scores = lax.dot_general(
            image_unit, text_from[k], (((1,), (1,)), ((), ())), preferred_element_type=jnp.float32
        )
        logits = multiplier_amount * scores + offset_value
        columns = source[k] * row_count + local
        pair_sign = jnp.where(label_rows[:, None] == columns[None, :], 1.0, -1.0).astype(
            jnp.float32
        )
        loss_local = loss_local + -jnp.sum(jax.nn.log_sigmoid(pair_sign * logits), axis=1)
        image_unit_grad = image_unit_grad + jnp.dot(
            weights_of(logits, pair_sign), text_from[k], preferred_element_type=jnp.float32
        )
    image_grad = (
        image_scale
        * (
            image_unit_grad
            - image_dir * jnp.sum(image_dir * image_unit_grad, axis=1, keepdims=True)
        )
    ).astype(jnp.bfloat16)
    return (loss_local[None], image_grad[None], projection_grad)


def solution(mesh):
    return jax.shard_map(
        body,
        mesh=mesh,
        in_specs=(
            P("group", "blk", None),
            P("group", "blk", None),
            P("group", None),
            P("group", "blk"),
            P(),
            P(),
        ),
        out_specs=(P("group", "blk"), P("group", "blk", None), P(("blk", "group"), None)),
        check_vma=False,
    )
```

```python
import jax
import jax.numpy as jnp
from jax import lax
from jax.sharding import PartitionSpec as P

epsilon = 1e-06


def partner_pairs(count, step):
    if count & (count - 1) == 0:
        return [(source, source ^ step) for source in range(count)]
    return [(source, (source + step) % count) for source in range(count)]


def partner_of(index, count, step):
    if count & (count - 1) == 0:
        return index ^ step
    return (index - step) % count


def body(
    picture_vector_list,
    caption_latent_matrix,
    linear_map_matrix,
    target_match_index,
    sharpness_factor,
    offset_term,
):
    image_rows = picture_vector_list[0]
    hidden_rows = caption_latent_matrix[0]
    label_rows = target_match_index[0]
    row_count = image_rows.shape[0]
    hid = hidden_rows.shape[1]
    blocks = lax.axis_size("blk")
    my_index = lax.axis_index("blk")
    chunk = hid // blocks
    multiplier_amount = sharpness_factor[0]
    offset_value = offset_term[0]

    def exchange(value, step):
        return lax.ppermute(value, "blk", partner_pairs(blocks, step))

    w_full = lax.all_gather(linear_map_matrix, "group", axis=0, tiled=True)

    image_float = image_rows.astype(jnp.float32)
    image_scale = lax.rsqrt(jnp.sum(image_float * image_float, axis=1, keepdims=True) + epsilon)
    image_dir = image_float * image_scale
    image_unit = image_dir.astype(jnp.bfloat16)

    source = [my_index] + [partner_of(my_index, blocks, k) for k in range(1, blocks)]
    own_hidden_chunk = lax.dynamic_slice_in_dim(hidden_rows, my_index * chunk, chunk, 1)
    hidden_from = [own_hidden_chunk]
    image_from = [image_unit]
    label_from = [label_rows]
    for k in range(1, blocks):
        target = partner_of(my_index, blocks, k)
        outgoing = jnp.concatenate(
            [lax.dynamic_slice_in_dim(hidden_rows, target * chunk, chunk, 1), image_unit], axis=1
        )
        incoming = exchange(outgoing, k)
        hidden_from.append(incoming[:, :chunk])
        image_from.append(incoming[:, chunk:])
        label_from.append(exchange(label_rows, k))

    projected = jnp.dot(hidden_rows, w_full, preferred_element_type=jnp.float32)
    text_scale = lax.rsqrt(jnp.sum(projected * projected, axis=1, keepdims=True) + epsilon)
    text_dir = projected * text_scale
    text_unit = text_dir.astype(jnp.bfloat16)
    text_from = [text_unit] + [exchange(text_unit, k) for k in range(1, blocks)]

    def weights_of(logits, pair_sign):
        return (-pair_sign * jax.nn.sigmoid(-pair_sign * logits) * multiplier_amount).astype(
            jnp.bfloat16
        )

    local = jnp.arange(row_count, dtype=jnp.int32)

    image_group = jnp.concatenate(image_from, axis=0)
    label_group = jnp.concatenate(label_from, axis=0)
    hidden_group = jnp.concatenate(hidden_from, axis=0)
    groups = lax.axis_size("group")
    parity = lax.axis_index("group") % 2
    owner_rows = chunk // groups
    by_owner = hidden_group.reshape(hidden_group.shape[0], groups // 2, 2, owner_rows)
    hidden_keep = lax.dynamic_index_in_dim(by_owner, parity, 2, keepdims=False).reshape(
        hidden_group.shape[0], chunk // 2
    )
    hidden_give = lax.dynamic_index_in_dim(by_owner, 1 - parity, 2, keepdims=False).reshape(
        hidden_group.shape[0], chunk // 2
    )
    own_columns = my_index * row_count + local
    scores_t = lax.dot_general(
        image_group, text_unit, (((1,), (1,)), ((), ())), preferred_element_type=jnp.float32
    )
    logits_t = multiplier_amount * scores_t + offset_value
    pair_sign_t = jnp.where(label_group[:, None] == own_columns[None, :], 1.0, -1.0).astype(
        jnp.float32
    )
    text_unit_grad = lax.dot_general(
        weights_of(logits_t, pair_sign_t),
        image_group,
        (((0,), (0,)), ((), ())),
        preferred_element_type=jnp.float32,
    )
    projection_output_gradient = (
        text_scale
        * (text_unit_grad - text_dir * jnp.sum(text_dir * text_unit_grad, axis=1, keepdims=True))
    ).astype(jnp.bfloat16)
    grad_from = [projection_output_gradient] + [
        exchange(projection_output_gradient, k) for k in range(1, blocks)
    ]
    grad_group = jnp.concatenate(grad_from, axis=0)

    def rows_for(hidden_part):
        return lax.dot_general(
            hidden_part, grad_group, (((0,), (0,)), ((), ())), preferred_element_type=jnp.float32
        ).reshape(groups // 2, owner_rows, grad_group.shape[1])
    mate_pairs = [(g, g ^ 1) for g in range(groups)]
    incoming = lax.ppermute(rows_for(hidden_give), "group", mate_pairs)
    chip_sum = rows_for(hidden_keep) + incoming
    same_core = [list(range(p, groups, 2)) for p in range(2)]
    projection_grad = lax.psum_scatter(
        chip_sum, "group", scatter_dimension=0, axis_index_groups=same_core, tiled=True
    ).reshape(owner_rows, grad_group.shape[1])

    loss_local = jnp.zeros((row_count,), jnp.float32)
    image_unit_grad = jnp.zeros(image_unit.shape, jnp.float32)
    for k in range(blocks):
        scores = lax.dot_general(
            image_unit, text_from[k], (((1,), (1,)), ((), ())), preferred_element_type=jnp.float32
        )
        logits = multiplier_amount * scores + offset_value
        columns = source[k] * row_count + local
        pair_sign = jnp.where(label_rows[:, None] == columns[None, :], 1.0, -1.0).astype(
            jnp.float32
        )
        loss_local = loss_local + -jnp.sum(jax.nn.log_sigmoid(pair_sign * logits), axis=1)
        image_unit_grad = image_unit_grad + jnp.dot(
            weights_of(logits, pair_sign), text_from[k], preferred_element_type=jnp.float32
        )
    image_grad = (
        image_scale
        * (
            image_unit_grad
            - image_dir * jnp.sum(image_dir * image_unit_grad, axis=1, keepdims=True)
        )
    ).astype(jnp.bfloat16)
    return (loss_local[None], image_grad[None], projection_grad)


def solution(mesh):
    return jax.shard_map(
        body,
        mesh=mesh,
        in_specs=(
            P("group", "blk", None),
            P("group", "blk", None),
            P("group", None),
            P("group", "blk"),
            P(),
            P(),
        ),
        out_specs=(P("group", "blk"), P("group", "blk", None), P(("blk", "group"), None)),
        check_vma=False,
    )
```

```python
import jax
import jax.numpy as jnp
from jax import lax
from jax.sharding import PartitionSpec as P

epsilon = 1e-06


def partner_pairs(count, step):
    if count & (count - 1) == 0:
        return [(source, source ^ step) for source in range(count)]
    return [(source, (source + step) % count) for source in range(count)]


def partner_of(index, count, step):
    if count & (count - 1) == 0:
        return index ^ step
    return (index - step) % count


def body(
    picture_vector_list,
    caption_latent_matrix,
    linear_map_matrix,
    target_match_index,
    sharpness_factor,
    offset_term,
):
    image_rows = picture_vector_list[0]
    hidden_rows = caption_latent_matrix[0]
    label_rows = target_match_index[0]
    row_count = image_rows.shape[0]
    hid = hidden_rows.shape[1]
    blocks = lax.axis_size("blk")
    my_index = lax.axis_index("blk")
    chunk = hid // blocks
    multiplier_amount = sharpness_factor[0]
    offset_value = offset_term[0]

    def exchange(value, step):
        return lax.ppermute(value, "blk", partner_pairs(blocks, step))

    groups = lax.axis_size("group")
    parity = lax.axis_index("group") % 2
    same_core = [list(range(p, groups, 2)) for p in range(2)]
    w_own = lax.all_gather(linear_map_matrix, "group", axis=0, axis_index_groups=same_core)
    shard_rows = linear_map_matrix.shape[0]
    hidden_by_shard = hidden_rows.reshape(hidden_rows.shape[0], groups // 2, 2, shard_rows)
    hidden_own = lax.dynamic_index_in_dim(hidden_by_shard, parity, 2, keepdims=False)
    hidden_mate = lax.dynamic_index_in_dim(hidden_by_shard, 1 - parity, 2, keepdims=False)

    image_float = image_rows.astype(jnp.float32)
    image_scale = lax.rsqrt(jnp.sum(image_float * image_float, axis=1, keepdims=True) + epsilon)
    image_dir = image_float * image_scale
    image_unit = image_dir.astype(jnp.bfloat16)

    source = [my_index] + [partner_of(my_index, blocks, k) for k in range(1, blocks)]
    own_hidden_chunk = lax.dynamic_slice_in_dim(hidden_rows, my_index * chunk, chunk, 1)
    hidden_from = [own_hidden_chunk]
    image_from = [image_unit]
    label_from = [label_rows]
    for k in range(1, blocks):
        target = partner_of(my_index, blocks, k)
        outgoing = jnp.concatenate(
            [lax.dynamic_slice_in_dim(hidden_rows, target * chunk, chunk, 1), image_unit], axis=1
        )
        incoming = exchange(outgoing, k)
        hidden_from.append(incoming[:, :chunk])
        image_from.append(incoming[:, chunk:])
        label_from.append(exchange(label_rows, k))

    contract = (((1, 2), (0, 1)), ((), ()))
    w_own, hidden_from, image_from, label_from = lax.optimization_barrier(
        (w_own, hidden_from, image_from, label_from)
    )
    w_mate = lax.ppermute(w_own, "group", [(g, g ^ 1) for g in range(groups)])
    projected = lax.dot_general(
        hidden_own, w_own, contract, preferred_element_type=jnp.float32
    ) + lax.dot_general(hidden_mate, w_mate, contract, preferred_element_type=jnp.float32)
    text_scale = lax.rsqrt(jnp.sum(projected * projected, axis=1, keepdims=True) + epsilon)
    text_dir = projected * text_scale
    text_unit = text_dir.astype(jnp.bfloat16)
    text_from = [text_unit] + [exchange(text_unit, k) for k in range(1, blocks)]

    def weights_of(logits, pair_sign):
        return (-pair_sign * jax.nn.sigmoid(-pair_sign * logits) * multiplier_amount).astype(
            jnp.bfloat16
        )

    local = jnp.arange(row_count, dtype=jnp.int32)

    image_group = jnp.concatenate(image_from, axis=0)
    label_group = jnp.concatenate(label_from, axis=0)
    hidden_group = jnp.concatenate(hidden_from, axis=0)
    own_columns = my_index * row_count + local
    scores_t = lax.dot_general(
        image_group, text_unit, (((1,), (1,)), ((), ())), preferred_element_type=jnp.float32
    )
    logits_t = multiplier_amount * scores_t + offset_value
    pair_sign_t = jnp.where(label_group[:, None] == own_columns[None, :], 1.0, -1.0).astype(
        jnp.float32
    )
    text_unit_grad = lax.dot_general(
        weights_of(logits_t, pair_sign_t),
        image_group,
        (((0,), (0,)), ((), ())),
        preferred_element_type=jnp.float32,
    )
    projection_output_gradient = (
        text_scale
        * (text_unit_grad - text_dir * jnp.sum(text_dir * text_unit_grad, axis=1, keepdims=True))
    ).astype(jnp.bfloat16)
    grad_from = [projection_output_gradient] + [
        exchange(projection_output_gradient, k) for k in range(1, blocks)
    ]
    partial = lax.dot_general(
        hidden_group,
        jnp.concatenate(grad_from, axis=0),
        (((0,), (0,)), ((), ())),
        preferred_element_type=jnp.float32,
    )
    projection_grad = lax.psum_scatter(partial, "group", scatter_dimension=0, tiled=True)

    loss_local = jnp.zeros((row_count,), jnp.float32)
    image_unit_grad = jnp.zeros(image_unit.shape, jnp.float32)
    for k in range(blocks):
        scores = lax.dot_general(
            image_unit, text_from[k], (((1,), (1,)), ((), ())), preferred_element_type=jnp.float32
        )
        logits = multiplier_amount * scores + offset_value
        columns = source[k] * row_count + local
        pair_sign = jnp.where(label_rows[:, None] == columns[None, :], 1.0, -1.0).astype(
            jnp.float32
        )
        loss_local = loss_local + -jnp.sum(jax.nn.log_sigmoid(pair_sign * logits), axis=1)
        image_unit_grad = image_unit_grad + jnp.dot(
            weights_of(logits, pair_sign), text_from[k], preferred_element_type=jnp.float32
        )
    image_grad = (
        image_scale
        * (
            image_unit_grad
            - image_dir * jnp.sum(image_dir * image_unit_grad, axis=1, keepdims=True)
        )
    ).astype(jnp.bfloat16)
    return (loss_local[None], image_grad[None], projection_grad)


def solution(mesh):
    return jax.shard_map(
        body,
        mesh=mesh,
        in_specs=(
            P("group", "blk", None),
            P("group", "blk", None),
            P("group", None),
            P("group", "blk"),
            P(),
            P(),
        ),
        out_specs=(P("group", "blk"), P("group", "blk", None), P(("blk", "group"), None)),
        check_vma=False,
    )
```

```python
import jax
import jax.numpy as jnp
from jax import lax
from jax.sharding import PartitionSpec as P

epsilon = 1e-06


def partner_pairs(count, step):
    if count & (count - 1) == 0:
        return [(source, source ^ step) for source in range(count)]
    return [(source, (source + step) % count) for source in range(count)]


def partner_of(index, count, step):
    if count & (count - 1) == 0:
        return index ^ step
    return (index - step) % count


def body(
    picture_vector_list,
    caption_latent_matrix,
    linear_map_matrix,
    target_match_index,
    sharpness_factor,
    offset_term,
):
    image_rows = picture_vector_list[0]
    hidden_rows = caption_latent_matrix[0]
    label_rows = target_match_index[0]
    row_count = image_rows.shape[0]
    hid = hidden_rows.shape[1]
    blocks = lax.axis_size("blk")
    my_index = lax.axis_index("blk")
    chunk = hid // blocks
    multiplier_amount = sharpness_factor[0]
    offset_value = offset_term[0]

    def exchange(value, step):
        return lax.ppermute(value, "blk", partner_pairs(blocks, step))

    w_full = lax.all_gather(linear_map_matrix, "group", axis=0, tiled=True)

    image_float = image_rows.astype(jnp.float32)
    image_scale = lax.rsqrt(jnp.sum(image_float * image_float, axis=1, keepdims=True) + epsilon)
    image_dir = image_float * image_scale
    image_unit = image_dir.astype(jnp.bfloat16)

    source = [my_index] + [partner_of(my_index, blocks, k) for k in range(1, blocks)]
    own_hidden_chunk = lax.dynamic_slice_in_dim(hidden_rows, my_index * chunk, chunk, 1)
    hidden_from = [own_hidden_chunk]
    image_from = [image_unit]
    label_from = [label_rows]
    for k in range(1, blocks):
        target = partner_of(my_index, blocks, k)
        outgoing = jnp.concatenate(
            [lax.dynamic_slice_in_dim(hidden_rows, target * chunk, chunk, 1), image_unit], axis=1
        )
        incoming = exchange(outgoing, k)
        hidden_from.append(incoming[:, :chunk])
        image_from.append(incoming[:, chunk:])
        label_from.append(exchange(label_rows, k))

    projected = jnp.dot(hidden_rows, w_full, preferred_element_type=jnp.float32)
    text_scale = lax.rsqrt(jnp.sum(projected * projected, axis=1, keepdims=True) + epsilon)
    text_dir = projected * text_scale
    text_unit = text_dir.astype(jnp.bfloat16)
    text_from = [text_unit] + [exchange(text_unit, k) for k in range(1, blocks)]

    def weights_of(logits, pair_sign):
        return (-pair_sign * jax.nn.sigmoid(-pair_sign * logits) * multiplier_amount).astype(
            jnp.bfloat16
        )

    local = jnp.arange(row_count, dtype=jnp.int32)

    image_group = jnp.concatenate(image_from, axis=0)
    label_group = jnp.concatenate(label_from, axis=0)
    hidden_rest = jnp.concatenate(hidden_from[1:], axis=0)
    own_columns = my_index * row_count + local
    scores_t = lax.dot_general(
        image_group, text_unit, (((1,), (1,)), ((), ())), preferred_element_type=jnp.float32
    )
    logits_t = multiplier_amount * scores_t + offset_value
    pair_sign_t = jnp.where(label_group[:, None] == own_columns[None, :], 1.0, -1.0).astype(
        jnp.float32
    )
    text_unit_grad = lax.dot_general(
        weights_of(logits_t, pair_sign_t),
        image_group,
        (((0,), (0,)), ((), ())),
        preferred_element_type=jnp.float32,
    )
    projection_output_gradient = (
        text_scale
        * (text_unit_grad - text_dir * jnp.sum(text_dir * text_unit_grad, axis=1, keepdims=True))
    ).astype(jnp.bfloat16)
    grad_from = [projection_output_gradient] + [
        exchange(projection_output_gradient, k) for k in range(1, blocks)
    ]
    contract_rows = (((0,), (0,)), ((), ()))
    partial = lax.dot_general(
        hidden_from[0], grad_from[0], contract_rows, preferred_element_type=jnp.float32
    ) + lax.dot_general(
        hidden_rest, jnp.concatenate(grad_from[1:], axis=0), contract_rows,
        preferred_element_type=jnp.float32,
    )
    projection_grad = lax.psum_scatter(partial, "group", scatter_dimension=0, tiled=True)

    loss_local = jnp.zeros((row_count,), jnp.float32)
    image_unit_grad = jnp.zeros(image_unit.shape, jnp.float32)
    for k in range(blocks):
        scores = lax.dot_general(
            image_unit, text_from[k], (((1,), (1,)), ((), ())), preferred_element_type=jnp.float32
        )
        logits = multiplier_amount * scores + offset_value
        columns = source[k] * row_count + local
        pair_sign = jnp.where(label_rows[:, None] == columns[None, :], 1.0, -1.0).astype(
            jnp.float32
        )
        loss_local = loss_local + -jnp.sum(jax.nn.log_sigmoid(pair_sign * logits), axis=1)
        image_unit_grad = image_unit_grad + jnp.dot(
            weights_of(logits, pair_sign), text_from[k], preferred_element_type=jnp.float32
        )
    image_grad = (
        image_scale
        * (
            image_unit_grad
            - image_dir * jnp.sum(image_dir * image_unit_grad, axis=1, keepdims=True)
        )
    ).astype(jnp.bfloat16)
    return (loss_local[None], image_grad[None], projection_grad)


def solution(mesh):
    return jax.shard_map(
        body,
        mesh=mesh,
        in_specs=(
            P("group", "blk", None),
            P("group", "blk", None),
            P("group", None),
            P("group", "blk"),
            P(),
            P(),
        ),
        out_specs=(P("group", "blk"), P("group", "blk", None), P(("blk", "group"), None)),
        check_vma=False,
    )
```

```python
import jax
import jax.numpy as jnp
from jax import lax
from jax.sharding import PartitionSpec as P

epsilon = 1e-06


def partner_pairs(count, step):
    if count & (count - 1) == 0:
        return [(source, source ^ step) for source in range(count)]
    return [(source, (source + step) % count) for source in range(count)]


def partner_of(index, count, step):
    if count & (count - 1) == 0:
        return index ^ step
    return (index - step) % count


def body(
    picture_vector_list,
    caption_latent_matrix,
    linear_map_matrix,
    target_match_index,
    sharpness_factor,
    offset_term,
):
    image_rows = picture_vector_list[0]
    hidden_rows = caption_latent_matrix[0]
    label_rows = target_match_index[0]
    row_count = image_rows.shape[0]
    hid = hidden_rows.shape[1]
    blocks = lax.axis_size("blk")
    my_index = lax.axis_index("blk")
    chunk = hid // blocks
    multiplier_amount = sharpness_factor[0]
    offset_value = offset_term[0]

    def exchange(value, step):
        return lax.ppermute(value, "blk", partner_pairs(blocks, step))

    w_full = lax.all_gather(linear_map_matrix, "group", axis=0, tiled=True)

    image_float = image_rows.astype(jnp.float32)
    image_scale = lax.rsqrt(jnp.sum(image_float * image_float, axis=1, keepdims=True) + epsilon)
    image_dir = image_float * image_scale
    image_unit = image_dir.astype(jnp.bfloat16)

    source = [my_index] + [partner_of(my_index, blocks, k) for k in range(1, blocks)]
    own_hidden_chunk = lax.dynamic_slice_in_dim(hidden_rows, my_index * chunk, chunk, 1)
    hidden_from = [own_hidden_chunk]
    image_from = [image_unit]
    label_from = [label_rows]
    for k in range(1, blocks):
        target = partner_of(my_index, blocks, k)
        outgoing = jnp.concatenate(
            [lax.dynamic_slice_in_dim(hidden_rows, target * chunk, chunk, 1), image_unit], axis=1
        )
        incoming = exchange(outgoing, k)
        hidden_from.append(incoming[:, :chunk])
        image_from.append(incoming[:, chunk:])
        label_from.append(exchange(label_rows, k))

    projected = jnp.dot(hidden_rows, w_full, preferred_element_type=jnp.float32)
    text_scale = lax.rsqrt(jnp.sum(projected * projected, axis=1, keepdims=True) + epsilon)
    text_dir = projected * text_scale
    text_unit = text_dir.astype(jnp.bfloat16)
    text_from = [text_unit] + [exchange(text_unit, k) for k in range(1, blocks)]

    def weights_of(logits, pair_sign):
        return (-pair_sign * jax.nn.sigmoid(-pair_sign * logits) * multiplier_amount).astype(
            jnp.bfloat16
        )

    local = jnp.arange(row_count, dtype=jnp.int32)

    image_group = jnp.concatenate(image_from, axis=0)
    label_group = jnp.concatenate(label_from, axis=0)
    hidden_natural = jnp.zeros((blocks,) + own_hidden_chunk.shape, own_hidden_chunk.dtype)
    for k in range(blocks):
        hidden_natural = lax.dynamic_update_slice_in_dim(
            hidden_natural, hidden_from[k][None], source[k], 0
        )
    hidden_group = hidden_natural.reshape(blocks * row_count, chunk)
    own_columns = my_index * row_count + local
    scores_t = lax.dot_general(
        image_group, text_unit, (((1,), (1,)), ((), ())), preferred_element_type=jnp.float32
    )
    logits_t = multiplier_amount * scores_t + offset_value
    pair_sign_t = jnp.where(label_group[:, None] == own_columns[None, :], 1.0, -1.0).astype(
        jnp.float32
    )
    text_unit_grad = lax.dot_general(
        weights_of(logits_t, pair_sign_t),
        image_group,
        (((0,), (0,)), ((), ())),
        preferred_element_type=jnp.float32,
    )
    projection_output_gradient = (
        text_scale
        * (text_unit_grad - text_dir * jnp.sum(text_dir * text_unit_grad, axis=1, keepdims=True))
    ).astype(jnp.bfloat16)
    partial = lax.dot_general(
        hidden_group,
        lax.all_gather(projection_output_gradient, "blk", axis=0, tiled=True),
        (((0,), (0,)), ((), ())),
        preferred_element_type=jnp.float32,
    )
    projection_grad = lax.psum_scatter(partial, "group", scatter_dimension=0, tiled=True)

    loss_local = jnp.zeros((row_count,), jnp.float32)
    image_unit_grad = jnp.zeros(image_unit.shape, jnp.float32)
    for k in range(blocks):
        scores = lax.dot_general(
            image_unit, text_from[k], (((1,), (1,)), ((), ())), preferred_element_type=jnp.float32
        )
        logits = multiplier_amount * scores + offset_value
        columns = source[k] * row_count + local
        pair_sign = jnp.where(label_rows[:, None] == columns[None, :], 1.0, -1.0).astype(
            jnp.float32
        )
        loss_local = loss_local + -jnp.sum(jax.nn.log_sigmoid(pair_sign * logits), axis=1)
        image_unit_grad = image_unit_grad + jnp.dot(
            weights_of(logits, pair_sign), text_from[k], preferred_element_type=jnp.float32
        )
    image_grad = (
        image_scale
        * (
            image_unit_grad
            - image_dir * jnp.sum(image_dir * image_unit_grad, axis=1, keepdims=True)
        )
    ).astype(jnp.bfloat16)
    return (loss_local[None], image_grad[None], projection_grad)


def solution(mesh):
    return jax.shard_map(
        body,
        mesh=mesh,
        in_specs=(
            P("group", "blk", None),
            P("group", "blk", None),
            P("group", None),
            P("group", "blk"),
            P(),
            P(),
        ),
        out_specs=(P("group", "blk"), P("group", "blk", None), P(("blk", "group"), None)),
        check_vma=False,
    )
```

```python
import jax
import jax.numpy as jnp
from jax import lax
from jax.sharding import PartitionSpec as P

epsilon = 1e-06


def partner_pairs(count, step):
    if count & (count - 1) == 0:
        return [(source, source ^ step) for source in range(count)]
    return [(source, (source + step) % count) for source in range(count)]


def partner_of(index, count, step):
    if count & (count - 1) == 0:
        return index ^ step
    return (index - step) % count


def body(
    picture_vector_list,
    caption_latent_matrix,
    linear_map_matrix,
    target_match_index,
    sharpness_factor,
    offset_term,
):
    image_rows = picture_vector_list[0]
    hidden_rows = caption_latent_matrix[0]
    label_rows = target_match_index[0]
    row_count = image_rows.shape[0]
    hid = hidden_rows.shape[1]
    blocks = lax.axis_size("blk")
    my_index = lax.axis_index("blk")
    chunk = hid // blocks
    multiplier_amount = sharpness_factor[0]
    offset_value = offset_term[0]

    def exchange(value, step):
        return lax.ppermute(value, "blk", partner_pairs(blocks, step))

    w_full = lax.all_gather(linear_map_matrix, "group", axis=0, tiled=True)

    image_float = image_rows.astype(jnp.float32)
    image_scale = lax.rsqrt(jnp.sum(image_float * image_float, axis=1, keepdims=True) + epsilon)
    image_dir = image_float * image_scale
    image_unit = image_dir.astype(jnp.bfloat16)

    source = [my_index] + [partner_of(my_index, blocks, k) for k in range(1, blocks)]
    own_hidden_chunk = lax.dynamic_slice_in_dim(hidden_rows, my_index * chunk, chunk, 1)
    hidden_from = [own_hidden_chunk]
    image_from = [image_unit]
    label_from = [label_rows]
    for k in range(1, blocks):
        target = partner_of(my_index, blocks, k)
        outgoing = jnp.concatenate(
            [lax.dynamic_slice_in_dim(hidden_rows, target * chunk, chunk, 1), image_unit], axis=1
        )
        incoming = exchange(outgoing, k)
        hidden_from.append(incoming[:, :chunk])
        image_from.append(incoming[:, chunk:])
        label_from.append(exchange(label_rows, k))

    projected = jnp.dot(hidden_rows, w_full, preferred_element_type=jnp.float32)
    text_scale = lax.rsqrt(jnp.sum(projected * projected, axis=1, keepdims=True) + epsilon)
    text_dir = projected * text_scale
    text_unit = text_dir.astype(jnp.bfloat16)
    text_from = [text_unit] + [exchange(text_unit, k) for k in range(1, blocks)]

    def weights_of(logits, pair_sign):
        return (-pair_sign * jax.nn.sigmoid(-pair_sign * logits) * multiplier_amount).astype(
            jnp.bfloat16
        )

    local = jnp.arange(row_count, dtype=jnp.int32)

    image_group = jnp.concatenate(image_from, axis=0)
    label_group = jnp.concatenate(label_from, axis=0)
    hidden_group = jnp.concatenate(hidden_from, axis=0)
    groups = lax.axis_size("group")
    parity = lax.axis_index("group") % 2
    owner_rows = chunk // groups
    mate_pairs = [(g, g ^ 1) for g in range(groups)]
    by_owner = hidden_group.reshape(hidden_group.shape[0], groups // 2, 2, owner_rows)
    hidden_keep = lax.dynamic_index_in_dim(by_owner, parity, 2, keepdims=False).reshape(
        hidden_group.shape[0], chunk // 2
    )
    hidden_give = lax.dynamic_index_in_dim(by_owner, 1 - parity, 2, keepdims=False).reshape(
        hidden_group.shape[0], chunk // 2
    )
    hidden_mate = lax.ppermute(hidden_give, "group", mate_pairs)
    own_columns = my_index * row_count + local
    scores_t = lax.dot_general(
        image_group, text_unit, (((1,), (1,)), ((), ())), preferred_element_type=jnp.float32
    )
    logits_t = multiplier_amount * scores_t + offset_value
    pair_sign_t = jnp.where(label_group[:, None] == own_columns[None, :], 1.0, -1.0).astype(
        jnp.float32
    )
    text_unit_grad = lax.dot_general(
        weights_of(logits_t, pair_sign_t),
        image_group,
        (((0,), (0,)), ((), ())),
        preferred_element_type=jnp.float32,
    )
    projection_output_gradient = (
        text_scale
        * (text_unit_grad - text_dir * jnp.sum(text_dir * text_unit_grad, axis=1, keepdims=True))
    ).astype(jnp.bfloat16)
    grad_send, hidden_keep, hidden_mate = lax.optimization_barrier(
        (projection_output_gradient, hidden_keep, hidden_mate)
    )
    grad_from = [projection_output_gradient] + [exchange(grad_send, k) for k in range(1, blocks)]
    grad_group = jnp.concatenate(grad_from, axis=0)
    grad_mate = lax.ppermute(grad_group, "group", mate_pairs)
    contract_rows = (((0,), (0,)), ((), ()))
    chip_sum = lax.dot_general(
        hidden_keep, grad_group, contract_rows, preferred_element_type=jnp.float32
    ) + lax.dot_general(hidden_mate, grad_mate, contract_rows, preferred_element_type=jnp.float32)
    same_core = [list(range(p, groups, 2)) for p in range(2)]
    projection_grad = lax.psum_scatter(
        chip_sum.reshape(groups // 2, owner_rows, grad_group.shape[1]),
        "group",
        scatter_dimension=0,
        axis_index_groups=same_core,
        tiled=True,
    ).reshape(owner_rows, grad_group.shape[1])

    loss_local = jnp.zeros((row_count,), jnp.float32)
    image_unit_grad = jnp.zeros(image_unit.shape, jnp.float32)
    for k in range(blocks):
        scores = lax.dot_general(
            image_unit, text_from[k], (((1,), (1,)), ((), ())), preferred_element_type=jnp.float32
        )
        logits = multiplier_amount * scores + offset_value
        columns = source[k] * row_count + local
        pair_sign = jnp.where(label_rows[:, None] == columns[None, :], 1.0, -1.0).astype(
            jnp.float32
        )
        loss_local = loss_local + -jnp.sum(jax.nn.log_sigmoid(pair_sign * logits), axis=1)
        image_unit_grad = image_unit_grad + jnp.dot(
            weights_of(logits, pair_sign), text_from[k], preferred_element_type=jnp.float32
        )
    image_grad = (
        image_scale
        * (
            image_unit_grad
            - image_dir * jnp.sum(image_dir * image_unit_grad, axis=1, keepdims=True)
        )
    ).astype(jnp.bfloat16)
    return (loss_local[None], image_grad[None], projection_grad)


def solution(mesh):
    return jax.shard_map(
        body,
        mesh=mesh,
        in_specs=(
            P("group", "blk", None),
            P("group", "blk", None),
            P("group", None),
            P("group", "blk"),
            P(),
            P(),
        ),
        out_specs=(P("group", "blk"), P("group", "blk", None), P(("blk", "group"), None)),
        check_vma=False,
    )
```
